1024 devices in a mesh: tensor: 16 (over x, y_lo), context: 32 (over z, y_hi), dp: 2 (over core).
Axes of the slice: x: 4, y: 8 (y_hi: 2, y_lo: 4; y = y_hi * 4 + y_lo), z: 16, core: 2. Of those that a mesh axis runs over, the one named last changes fastest.
Arguments:
- tokens: bfloat16 [2, 32, 128, 8192], P('dp', 'context', 'tensor'), may hold values from -6 to 6
- w_in: bfloat16 [8192, 2, 4096], P(None, None, 'tensor'), may hold values from -0.0625 to 0.0625
- gate: bfloat16 [2, 32, 128, 4096], P('dp', 'context', None, 'tensor'), may hold values from -6 to 6
- cotangent: bfloat16 [2, 32, 128, 4096], P('dp', 'context', None, 'tensor'), may hold values from -6 to 6
- filters: bfloat16 [256, 128], P('tensor'), may hold values from -0.5 to 0.5
Outputs:
- d_tokens: bfloat16 [2, 32, 128, 8192], P('dp', 'context', 'tensor')
- d_gate: bfloat16 [2, 32, 128, 4096], P('dp', 'context', None, 'tensor')
- d_filter: float32 [256, 128], P('tensor')
The draws below stay inside these ranges and needn't reach their ends.
All inputs are finite; a program needn't handle non-finite values.
Results may differ from the reference program's by a relative error of at most 0.018.
Values may be sent and summed in bfloat16 or wider, within the bound.
No kernel may reach another device: no remote copies, remote signals or barrier semaphores. Data moves between devices by JAX's collectives and lax.ppermute only.
A program may use at most 64 MiB of HBM per device.

```python
import math
import jax
import jax.numpy as jnp
from jax import lax

D = 8192
WC = 4096
GS = 16
KLEN = 128
STRETCH = 128
SEQS = 2
NCH = 32
LEN = 4096
GROUPS = 256
N_TENSOR = 16


def shard_levels(rng, extent, split, least, largest):
    loudness, own = 1.0, jax.random.fold_in(rng, 6)
    for dim, shards_of in split:
        draws = jnp.exp(jax.random.uniform(jax.random.fold_in(own, dim), (shards_of,), jnp.float32, least / len(split), largest / len(split)))
        loudness = loudness * jnp.repeat(draws, extent[dim] // shards_of).reshape([-1 if axis == dim else 1 for axis in range(len(extent))])
    return loudness


def bell_draw(key, extent, scale, most, pieces=(), kind=jnp.bfloat16):
    values = scale * jax.random.normal(key, extent, jnp.float32)
    if pieces:
        values = values * shard_levels(key, extent, pieces, -0.22, 0.18)
    return jnp.clip(values, -most, most).astype(kind)


def setup_inputs(seed: int = 0) -> dict:
    key_list = jax.random.split(jax.random.key(seed), 6)
    tokens = bell_draw(key_list[0], (SEQS, NCH, STRETCH, D), 1.0, 6.0, ((0, 2), (1, 32), (2, 16)))
    w_in = bell_draw(key_list[1], (D, 2, WC), D ** -0.5, 0.0625, ((2, 16),))
    gate = bell_draw(key_list[2], (SEQS, NCH, STRETCH, WC), 1.0, 6.0, ((0, 2), (1, 32), (3, 16)))
    cotangent = bell_draw(key_list[3], (SEQS, NCH, STRETCH, WC), 1.0, 6.0, ((0, 2), (1, 32), (3, 16)))
    filters = bell_draw(key_list[4], (GROUPS, KLEN), KLEN ** -0.5, 0.5, ((0, 16),))
    return dict(tokens=tokens, w_in=w_in, gate=gate, cotangent=cotangent, filters=filters)


def reference(tokens, w_in, gate, cotangent, filters):
    weight_flat = w_in.reshape(D, 2 * WC)
    all_rows = tokens.reshape(SEQS * LEN, D)
    projected = jnp.dot(all_rows, weight_flat, preferred_element_type=jnp.float32).astype(jnp.bfloat16)
    projected = projected.reshape(SEQS, LEN, 2, WC)
    second_in = projected[:, :, 0].astype(jnp.float32)
    value_in = projected[:, :, 1].astype(jnp.float32)
    mixed = lax.optimization_barrier((second_in * value_in).astype(jnp.bfloat16)).astype(jnp.float32)
    tap_table = jnp.repeat(filters.astype(jnp.float32), GS, axis=0)
    gate_full = gate.reshape(SEQS, LEN, WC).astype(jnp.float32)
    grad_out = cotangent.reshape(SEQS, LEN, WC).astype(jnp.float32)
    mixed_pad = jnp.pad(mixed, ((0, 0), (KLEN, 0), (0, 0)))

    def conv_step(step, acc):
        step = jnp.asarray(step).astype(jnp.int32)
        window = lax.dynamic_slice_in_dim(mixed_pad, (KLEN - step).astype(jnp.int32), LEN, 1)
        return acc + window * lax.dynamic_index_in_dim(tap_table, step, 1, keepdims=False)
    conv_out = lax.fori_loop(0, KLEN, conv_step, jnp.zeros((SEQS, LEN, WC), jnp.float32))
    d_gate = (grad_out * conv_out).astype(jnp.bfloat16).reshape(SEQS, NCH, STRETCH, WC)
    grad_mix = lax.optimization_barrier((grad_out * gate_full).astype(jnp.bfloat16)).astype(jnp.float32)
    grad_pad = jnp.pad(grad_mix, ((0, 0), (0, KLEN), (0, 0)))

    def back_step(step, acc):
        step = jnp.asarray(step).astype(jnp.int32)
        window = lax.dynamic_slice_in_dim(grad_pad, step, LEN, 1)
        return acc + window * lax.dynamic_index_in_dim(tap_table, step, 1, keepdims=False)
    grad_conv = lax.fori_loop(0, KLEN, back_step, jnp.zeros((SEQS, LEN, WC), jnp.float32))
    grad_in = jnp.stack([grad_conv * value_in, grad_conv * second_in], axis=2).astype(jnp.bfloat16)
    local_width = WC // N_TENSOR
    grad_sets = grad_in.reshape(SEQS * LEN, 2, N_TENSOR, local_width)
    weight_sets = w_in.reshape(D, 2, N_TENSOR, local_width)

    def shard_step(index, acc):
        index = jnp.asarray(index).astype(jnp.int32)
        grad_piece = lax.dynamic_index_in_dim(grad_sets, index, 2, keepdims=False).reshape(SEQS * LEN, 2 * local_width)
        weight_piece = lax.dynamic_index_in_dim(weight_sets, index, 2, keepdims=False).reshape(D, 2 * local_width)
        partial_value = lax.dot_general(grad_piece, weight_piece, (((1,), (1,)), ((), ())), preferred_element_type=jnp.float32)
        rounded = lax.optimization_barrier(partial_value.astype(jnp.bfloat16)).astype(jnp.float32)
        return acc + rounded
    d_tokens = lax.fori_loop(0, N_TENSOR, shard_step, jnp.zeros((SEQS * LEN, D), jnp.float32))
    d_tokens = d_tokens.astype(jnp.bfloat16).reshape(SEQS, NCH, STRETCH, D)

    def filter_term(step):
        step = step.astype(jnp.int32)
        window = lax.dynamic_slice_in_dim(mixed_pad, (KLEN - step).astype(jnp.int32), LEN, 1)
        per_channel = lax.optimization_barrier(jnp.sum(grad_mix * window, axis=(0, 1)))
        return per_channel.reshape(GROUPS, GS).sum(axis=1)
    filter_sums = lax.map(filter_term, jnp.arange(KLEN, dtype=jnp.int32))
    d_filter = filter_sums.T * (1.0 / math.sqrt(SEQS * LEN * GS))
    return (d_tokens, d_gate, d_filter.astype(jnp.float32))
```

```python
import math

import jax
import jax.numpy as jnp
from jax import lax
from jax.sharding import PartitionSpec as P


def from_behind(value, axis, steps):
    count = lax.axis_size(axis)
    first, last = (max(0, -steps), min(count, count - steps))
    return lax.ppermute(value, axis, [(source, source + steps) for source in range(first, last)])


def butterfly_sum(value, axis):
    count = lax.axis_size(axis)
    if count & (count - 1):
        return lax.psum(value, axis)
    step = 1
    while step < count:
        value = value + lax.ppermute(value, axis, [(i, i ^ step) for i in range(count)])
        step *= 2
    return value


def skew_band(filters, stretch_rows):
    groups, tap_count = filters.shape
    band_width = stretch_rows + tap_count
    reversed_taps = filters[:, ::-1]
    pattern = jnp.concatenate(
        [
            jnp.zeros((groups, 1), filters.dtype),
            reversed_taps,
            jnp.zeros((groups, stretch_rows), filters.dtype),
        ],
        axis=1,
    )
    tiled = jnp.tile(pattern, (1, stretch_rows))[:, : stretch_rows * band_width]
    return tiled.reshape(groups, stretch_rows, band_width)


def band_sums(products, tap_count):
    groups, stretch_rows, band_width = products.shape
    flat_view = jnp.pad(
        products.reshape(groups, stretch_rows * band_width), ((0, 0), (0, stretch_rows))
    )
    folded = flat_view.reshape(groups, stretch_rows, band_width + 1).sum(axis=1)
    return folded[:, tap_count:0:-1]


def body(tokens, w_in, gate, cotangent, filters):
    seq_count = tokens.shape[0]
    model_width = tokens.shape[3]
    channels = w_in.shape[2]
    groups, tap_count = filters.shape
    group_size = channels // groups
    stretch_rows = gate.shape[2]
    weight_flat = w_in.reshape(model_width, 2 * channels)
    projected = jnp.einsum(
        "abnd,dc->abnc",
        lax.all_gather(tokens, "tensor", axis=2, tiled=True),
        weight_flat,
        preferred_element_type=jnp.float32,
    ).astype(jnp.bfloat16)[:, 0]
    second_in = projected[..., :channels].astype(jnp.float32)
    value_in = projected[..., channels:].astype(jnp.float32)
    mixed = (second_in * value_in).astype(jnp.bfloat16)
    gate_rows = gate[:, 0].astype(jnp.float32)
    grad_out = cotangent[:, 0].astype(jnp.float32)
    grad_mix = (grad_out * gate_rows).astype(jnp.bfloat16)
    prev_rows = from_behind(mixed[:, stretch_rows - (tap_count - 1) :], "context", 1)
    extended = jnp.concatenate(
        [jnp.zeros((seq_count, 1, channels), jnp.bfloat16), prev_rows, mixed], axis=1
    )
    extended = extended.reshape(seq_count, stretch_rows + tap_count, groups, group_size)
    toeplitz = skew_band(filters, stretch_rows)
    conv_out = jnp.einsum("gts,bsgc->btgc", toeplitz, extended, preferred_element_type=jnp.float32)
    conv_out = conv_out.reshape(seq_count, stretch_rows, channels)
    d_gate = (grad_out * conv_out).astype(jnp.bfloat16)[:, None]
    grad_blocks = grad_mix.reshape(seq_count, stretch_rows, groups, group_size)
    spread = jnp.einsum("gts,btgc->bsgc", toeplitz, grad_blocks, preferred_element_type=jnp.float32)
    own_part = spread[:, tap_count:]
    next_rows_in = from_behind(grad_mix[:, : tap_count - 1], "context", -1)
    next_blocks = next_rows_in.reshape(seq_count, tap_count - 1, groups, group_size)
    from_next = jnp.einsum(
        "gts,btgc->bsgc",
        toeplitz[:, : tap_count - 1, 1:tap_count],
        next_blocks,
        preferred_element_type=jnp.float32,
    )
    split_at = stretch_rows - tap_count + 1
    grad_conv = jnp.concatenate(
        [own_part[:, :split_at], own_part[:, split_at:] + from_next], axis=1
    )
    grad_conv = grad_conv.reshape(seq_count, stretch_rows, channels)
    grad_in = jnp.concatenate([grad_conv * value_in, grad_conv * second_in], axis=-1).astype(
        jnp.bfloat16
    )
    partials = jnp.einsum("bnc,dc->bnd", grad_in, weight_flat, preferred_element_type=jnp.float32)
    d_tokens = lax.psum_scatter(
        partials.astype(jnp.bfloat16), "tensor", scatter_dimension=1, tiled=True
    ).astype(jnp.float32)
    d_tokens = d_tokens.astype(jnp.bfloat16)[:, None]
    products = jnp.einsum(
        "btgc,bsgc->gts", grad_blocks, extended, preferred_element_type=jnp.float32
    )
    local_grad = band_sums(products, tap_count)
    summed = butterfly_sum(butterfly_sum(local_grad, "dp"), "context")
    term_total = (
        seq_count * lax.axis_size("dp") * stretch_rows * lax.axis_size("context") * group_size
    )
    d_filter = summed * (1.0 / math.sqrt(term_total))
    return (d_tokens, d_gate, d_filter)


def solution(mesh):
    return jax.shard_map(
        body,
        mesh=mesh,
        in_specs=(
            P("dp", "context", "tensor", None),
            P(None, None, "tensor"),
            P("dp", "context", None, "tensor"),
            P("dp", "context", None, "tensor"),
            P("tensor", None),
        ),
        out_specs=(
            P("dp", "context", "tensor", None),
            P("dp", "context", None, "tensor"),
            P("tensor", None),
        ),
        check_vma=False,
    )
```

```python
import math

import jax
import jax.numpy as jnp
from jax import lax
from jax.sharding import PartitionSpec as P


def from_behind(value, axis, steps):
    count = lax.axis_size(axis)
    first, last = (max(0, -steps), min(count, count - steps))
    return lax.ppermute(value, axis, [(source, source + steps) for source in range(first, last)])


def butterfly_sum(value, axis):
    count = lax.axis_size(axis)
    if count & (count - 1):
        return lax.psum(value, axis)
    step = 1
    while step < count:
        value = value + lax.ppermute(value, axis, [(i, i ^ step) for i in range(count)])
        step *= 2
    return value


def grid_shift(axis, steps, inner, outer_step):
    count = lax.axis_size(axis)
    if outer_step:
        return [(i, ((i // inner + steps) % (count // inner)) * inner + i % inner) for i in range(count)]
    return [(i, (i // inner) * inner + (i % inner + steps) % inner) for i in range(count)]


def grid_gather(rows, axis, inner):
    count = lax.axis_size(axis)
    outer = count // inner
    index = lax.axis_index(axis)
    pieces = [rows] + [
        lax.ppermute(rows, axis, grid_shift(axis, s, inner, False)) for s in range(1, inner)
    ]
    order = (index % inner - jnp.arange(inner)) % inner
    stage = jnp.take(jnp.stack(pieces), order, axis=0)
    pieces = [stage] + [
        lax.ppermute(stage, axis, grid_shift(axis, s, inner, True)) for s in range(1, outer)
    ]
    order = (index // inner - jnp.arange(outer)) % outer
    return jnp.take(jnp.stack(pieces), order, axis=0).reshape((count * rows.shape[0],) + rows.shape[1:])


def grid_reduce_scatter(partial_rows, axis, inner):
    count = lax.axis_size(axis)
    outer = count // inner
    index = lax.axis_index(axis)
    chunks = partial_rows.reshape((outer, -1) + partial_rows.shape[1:])
    acc = jnp.take(chunks, index // inner, axis=0).astype(jnp.float32)
    for s in range(1, outer):
        sent = jnp.take(chunks, (index // inner + s) % outer, axis=0)
        acc = acc + lax.ppermute(sent, axis, grid_shift(axis, s, inner, True)).astype(jnp.float32)
    chunks = acc.reshape((inner, -1) + acc.shape[1:])
    total = jnp.take(chunks, index % inner, axis=0)
    for s in range(1, inner):
        sent = jnp.take(chunks, (index % inner + s) % inner, axis=0)
        total = total + lax.ppermute(sent, axis, grid_shift(axis, s, inner, False))
    return total


def skew_band(filters, stretch_rows):
    groups, tap_count = filters.shape
    band_width = stretch_rows + tap_count
    reversed_taps = filters[:, ::-1]
    pattern = jnp.concatenate(
        [
            jnp.zeros((groups, 1), filters.dtype),
            reversed_taps,
            jnp.zeros((groups, stretch_rows), filters.dtype),
        ],
        axis=1,
    )
    tiled = jnp.tile(pattern, (1, stretch_rows))[:, : stretch_rows * band_width]
    return tiled.reshape(groups, stretch_rows, band_width)


def band_sums(products, tap_count):
    groups, stretch_rows, band_width = products.shape
    flat_view = jnp.pad(
        products.reshape(groups, stretch_rows * band_width), ((0, 0), (0, stretch_rows))
    )
    folded = flat_view.reshape(groups, stretch_rows, band_width + 1).sum(axis=1)
    return folded[:, tap_count:0:-1]


def body(tokens, w_in, gate, cotangent, filters):
    seq_count = tokens.shape[0]
    model_width = tokens.shape[3]
    channels = w_in.shape[2]
    groups, tap_count = filters.shape
    group_size = channels // groups
    stretch_rows = gate.shape[2]
    weight_flat = w_in.reshape(model_width, 2 * channels)
    inner = 4 if lax.axis_size("tensor") % 4 == 0 else 1
    block_rows = grid_gather(tokens.reshape(tokens.shape[2], model_width), "tensor", inner)
    projected = jnp.einsum(
        "nd,dc->nc", block_rows, weight_flat, preferred_element_type=jnp.float32
    ).astype(jnp.bfloat16)[None]
    second_in = projected[..., :channels].astype(jnp.float32)
    value_in = projected[..., channels:].astype(jnp.float32)
    mixed = (second_in * value_in).astype(jnp.bfloat16)
    gate_rows = gate[:, 0].astype(jnp.float32)
    grad_out = cotangent[:, 0].astype(jnp.float32)
    grad_mix = (grad_out * gate_rows).astype(jnp.bfloat16)
    prev_rows = from_behind(mixed[:, stretch_rows - (tap_count - 1) :], "context", 1)
    extended = jnp.concatenate(
        [jnp.zeros((seq_count, 1, channels), jnp.bfloat16), prev_rows, mixed], axis=1
    )
    extended = extended.reshape(seq_count, stretch_rows + tap_count, groups, group_size)
    toeplitz = skew_band(filters, stretch_rows)
    conv_out = jnp.einsum("gts,bsgc->btgc", toeplitz, extended, preferred_element_type=jnp.float32)
    conv_out = conv_out.reshape(seq_count, stretch_rows, channels)
    d_gate = (grad_out * conv_out).astype(jnp.bfloat16)[:, None]
    grad_blocks = grad_mix.reshape(seq_count, stretch_rows, groups, group_size)
    spread = jnp.einsum("gts,btgc->bsgc", toeplitz, grad_blocks, preferred_element_type=jnp.float32)
    own_part = spread[:, tap_count:]
    next_rows_in = from_behind(grad_mix[:, : tap_count - 1], "context", -1)
    next_blocks = next_rows_in.reshape(seq_count, tap_count - 1, groups, group_size)
    from_next = jnp.einsum(
        "gts,btgc->bsgc",
        toeplitz[:, : tap_count - 1, 1:tap_count],
        next_blocks,
        preferred_element_type=jnp.float32,
    )
    split_at = stretch_rows - tap_count + 1
    grad_conv = jnp.concatenate(
        [own_part[:, :split_at], own_part[:, split_at:] + from_next], axis=1
    )
    grad_conv = grad_conv.reshape(seq_count, stretch_rows, channels)
    grad_in = jnp.concatenate([grad_conv * value_in, grad_conv * second_in], axis=-1).astype(
        jnp.bfloat16
    )
    partials = jnp.einsum("bnc,dc->bnd", grad_in, weight_flat, preferred_element_type=jnp.float32)
    d_tokens = grid_reduce_scatter(partials[0].astype(jnp.bfloat16), "tensor", inner)
    d_tokens = d_tokens.astype(jnp.bfloat16)[None, None]
    products = jnp.einsum(
        "btgc,bsgc->gts", grad_blocks, extended, preferred_element_type=jnp.float32
    )
    local_grad = band_sums(products, tap_count)
    summed = butterfly_sum(butterfly_sum(local_grad, "dp"), "context")
    term_total = (
        seq_count * lax.axis_size("dp") * stretch_rows * lax.axis_size("context") * group_size
    )
    d_filter = summed * (1.0 / math.sqrt(term_total))
    return (d_tokens, d_gate, d_filter)


def solution(mesh):
    return jax.shard_map(
        body,
        mesh=mesh,
        in_specs=(
            P("dp", "context", "tensor", None),
            P(None, None, "tensor"),
            P("dp", "context", None, "tensor"),
            P("dp", "context", None, "tensor"),
            P("tensor", None),
        ),
        out_specs=(
            P("dp", "context", "tensor", None),
            P("dp", "context", None, "tensor"),
            P("tensor", None),
        ),
        check_vma=False,
    )
```

```python
import math

import jax
import jax.numpy as jnp
from jax import lax
from jax.sharding import PartitionSpec as P


def from_behind(value, axis, steps):
    count = lax.axis_size(axis)
    first, last = (max(0, -steps), min(count, count - steps))
    return lax.ppermute(value, axis, [(source, source + steps) for source in range(first, last)])


def butterfly_sum(value, axis):
    count = lax.axis_size(axis)
    if count & (count - 1):
        return lax.psum(value, axis)
    step = 1
    while step < count:
        value = value + lax.ppermute(value, axis, [(i, i ^ step) for i in range(count)])
        step *= 2
    return value


def grid_shift(axis, steps, inner, outer_step):
    count = lax.axis_size(axis)
    if outer_step:
        return [(i, ((i // inner + steps) % (count // inner)) * inner + i % inner) for i in range(count)]
    return [(i, (i // inner) * inner + (i % inner + steps) % inner) for i in range(count)]


def grid_gather(rows, axis, inner):
    count = lax.axis_size(axis)
    outer = count // inner
    index = lax.axis_index(axis)
    pieces = [rows] + [
        lax.ppermute(rows, axis, grid_shift(axis, s, inner, False)) for s in range(1, inner)
    ]
    order = (index % inner - jnp.arange(inner)) % inner
    stage = jnp.take(jnp.stack(pieces), order, axis=0)
    pieces = [stage] + [
        lax.ppermute(stage, axis, grid_shift(axis, s, inner, True)) for s in range(1, outer)
    ]
    order = (index // inner - jnp.arange(outer)) % outer
    return jnp.take(jnp.stack(pieces), order, axis=0).reshape((count * rows.shape[0],) + rows.shape[1:])


def grid_reduce_scatter(partial_rows, axis, inner):
    count = lax.axis_size(axis)
    outer = count // inner
    index = lax.axis_index(axis)
    chunks = partial_rows.reshape((outer, -1) + partial_rows.shape[1:])
    acc = jnp.take(chunks, index // inner, axis=0).astype(jnp.float32)
    for s in range(1, outer):
        sent = jnp.take(chunks, (index // inner + s) % outer, axis=0)
        acc = acc + lax.ppermute(sent, axis, grid_shift(axis, s, inner, True)).astype(jnp.float32)
    chunks = acc.reshape((inner, -1) + acc.shape[1:])
    total = jnp.take(chunks, index % inner, axis=0)
    for s in range(1, inner):
        sent = jnp.take(chunks, (index % inner + s) % inner, axis=0)
        total = total + lax.ppermute(sent, axis, grid_shift(axis, s, inner, False))
    return total


def skew_band(filters, stretch_rows):
    groups, tap_count = filters.shape
    band_width = stretch_rows + tap_count
    reversed_taps = filters[:, ::-1]
    pattern = jnp.concatenate(
        [
            jnp.zeros((groups, 1), filters.dtype),
            reversed_taps,
            jnp.zeros((groups, stretch_rows), filters.dtype),
        ],
        axis=1,
    )
    tiled = jnp.tile(pattern, (1, stretch_rows))[:, : stretch_rows * band_width]
    return tiled.reshape(groups, stretch_rows, band_width)


def band_sums(products, tap_count):
    groups, stretch_rows, band_width = products.shape
    flat_view = jnp.pad(
        products.reshape(groups, stretch_rows * band_width), ((0, 0), (0, stretch_rows))
    )
    folded = flat_view.reshape(groups, stretch_rows, band_width + 1).sum(axis=1)
    return folded[:, tap_count:0:-1]


def band_sums_ahead(products, tap_count):
    groups, stretch_rows, band_width = products.shape
    flat_view = jnp.pad(
        products.reshape(groups, stretch_rows * band_width), ((0, 0), (0, stretch_rows))
    )
    folded = flat_view.reshape(groups, stretch_rows, band_width + 1).sum(axis=1)
    return folded[:, :tap_count]


def body(tokens, w_in, gate, cotangent, filters):
    seq_count = tokens.shape[0]
    model_width = tokens.shape[3]
    channels = w_in.shape[2]
    groups, tap_count = filters.shape
    group_size = channels // groups
    stretch_rows = gate.shape[2]
    weight_flat = w_in.reshape(model_width, 2 * channels)
    inner = 4 if lax.axis_size("tensor") % 4 == 0 else 1
    block_rows = grid_gather(tokens.reshape(tokens.shape[2], model_width), "tensor", inner)
    projected = jnp.einsum(
        "nd,djc->njc", block_rows, w_in, preferred_element_type=jnp.float32
    ).astype(jnp.bfloat16).reshape(1, block_rows.shape[0], 2 * channels)
    second_in = projected[..., :channels].astype(jnp.float32)
    value_in = projected[..., channels:].astype(jnp.float32)
    mixed = (second_in * value_in).astype(jnp.bfloat16)
    gate_rows = gate[:, 0].astype(jnp.float32)
    grad_out = cotangent[:, 0].astype(jnp.float32)
    grad_mix = (grad_out * gate_rows).astype(jnp.bfloat16)
    prev_rows = from_behind(mixed[:, stretch_rows - (tap_count - 1) :], "context", 1)
    extended = jnp.concatenate(
        [jnp.zeros((seq_count, 1, channels), jnp.bfloat16), prev_rows, mixed], axis=1
    )
    extended = extended.reshape(seq_count, stretch_rows + tap_count, groups, group_size)
    toeplitz = skew_band(filters, stretch_rows)
    conv_out = jnp.einsum("gts,bsgc->btgc", toeplitz, extended, preferred_element_type=jnp.float32)
    conv_out = conv_out.reshape(seq_count, stretch_rows, channels)
    d_gate = (grad_out * conv_out).astype(jnp.bfloat16)[:, None]
    grad_blocks = grad_mix.reshape(seq_count, stretch_rows, groups, group_size)
    spread = jnp.einsum("gts,btgc->bsgc", toeplitz, grad_blocks, preferred_element_type=jnp.float32)
    own_part = spread[:, tap_count:]
    next_rows_in = from_behind(grad_mix[:, : tap_count - 1], "context", -1)
    next_blocks = next_rows_in.reshape(seq_count, tap_count - 1, groups, group_size)
    from_next = jnp.einsum(
        "gts,btgc->bsgc",
        toeplitz[:, : tap_count - 1, 1:tap_count],
        next_blocks,
        preferred_element_type=jnp.float32,
    )
    split_at = stretch_rows - tap_count + 1
    grad_conv = jnp.concatenate(
        [own_part[:, :split_at], own_part[:, split_at:] + from_next], axis=1
    )
    grad_conv = grad_conv.reshape(seq_count, stretch_rows, channels)
    grad_in = jnp.concatenate([grad_conv * value_in, grad_conv * second_in], axis=-1).astype(
        jnp.bfloat16
    )
    partials = jnp.einsum(
        "bnjc,djc->bnd",
        grad_in.reshape(grad_in.shape[:2] + (2, channels)),
        w_in,
        preferred_element_type=jnp.float32,
    )
    d_tokens = grid_reduce_scatter(partials[0].astype(jnp.bfloat16), "tensor", inner)
    d_tokens = d_tokens.astype(jnp.bfloat16)[None, None]
    grad_ahead = jnp.concatenate(
        [grad_mix, next_rows_in, jnp.zeros((seq_count, 1, channels), jnp.bfloat16)], axis=1
    ).reshape(seq_count, stretch_rows + tap_count, groups, group_size)
    products = jnp.einsum(
        "bsgc,btgc->gst",
        mixed.reshape(seq_count, stretch_rows, groups, group_size),
        grad_ahead,
        preferred_element_type=jnp.float32,
    )
    local_grad = band_sums_ahead(products, tap_count)
    summed = butterfly_sum(butterfly_sum(local_grad, "dp"), "context")
    term_total = (
        seq_count * lax.axis_size("dp") * stretch_rows * lax.axis_size("context") * group_size
    )
    d_filter = summed * (1.0 / math.sqrt(term_total))
    return (d_tokens, d_gate, d_filter)


def solution(mesh):
    return jax.shard_map(
        body,
        mesh=mesh,
        in_specs=(
            P("dp", "context", "tensor", None),
            P(None, None, "tensor"),
            P("dp", "context", None, "tensor"),
            P("dp", "context", None, "tensor"),
            P("tensor", None),
        ),
        out_specs=(
            P("dp", "context", "tensor", None),
            P("dp", "context", None, "tensor"),
            P("tensor", None),
        ),
        check_vma=False,
    )
```

```python
import math

import jax
import jax.numpy as jnp
from jax import lax
from jax.sharding import PartitionSpec as P


def from_behind(value, axis, steps):
    count = lax.axis_size(axis)
    first, last = (max(0, -steps), min(count, count - steps))
    return lax.ppermute(value, axis, [(source, source + steps) for source in range(first, last)])


def butterfly_sum(value, axis):
    count = lax.axis_size(axis)
    if count & (count - 1):
        return lax.psum(value, axis)
    step = 1
    while step < count:
        value = value + lax.ppermute(value, axis, [(i, i ^ step) for i in range(count)])
        step *= 2
    return value


def butterfly_rounds(value, axis, steps):
    count = lax.axis_size(axis)
    for step in steps:
        value = value + lax.ppermute(value, axis, [(i, i ^ step) for i in range(count)])
    return value


def grid_shift(axis, steps, inner, outer_step):
    count = lax.axis_size(axis)
    if outer_step:
        return [(i, ((i // inner + steps) % (count // inner)) * inner + i % inner) for i in range(count)]
    return [(i, (i // inner) * inner + (i % inner + steps) % inner) for i in range(count)]


def grid_gather(rows, axis, inner):
    count = lax.axis_size(axis)
    outer = count // inner
    index = lax.axis_index(axis)
    pieces = [rows] + [
        lax.ppermute(rows, axis, grid_shift(axis, s, inner, False)) for s in range(1, inner)
    ]
    order = (index % inner - jnp.arange(inner)) % inner
    stage = jnp.take(jnp.stack(pieces), order, axis=0)
    pieces = [stage] + [
        lax.ppermute(stage, axis, grid_shift(axis, s, inner, True)) for s in range(1, outer)
    ]
    order = (index // inner - jnp.arange(outer)) % outer
    return jnp.take(jnp.stack(pieces), order, axis=0).reshape((count * rows.shape[0],) + rows.shape[1:])


def scatter_stage(chunks, axis, inner, outer_step, wide):
    count = lax.axis_size(axis)
    size = count // inner if outer_step else inner
    index = lax.axis_index(axis)
    place = index // inner if outer_step else index % inner
    acc = jnp.take(chunks, place, axis=0).astype(jnp.float32)
    for s in range(1, size):
        sent = jnp.take(chunks, (place + s) % size, axis=0)
        if wide:
            sent = sent.astype(jnp.float32)
        acc = acc + lax.ppermute(sent, axis, grid_shift(axis, s, inner, outer_step)).astype(jnp.float32)
    return acc


def skew_band(filters, stretch_rows):
    groups, tap_count = filters.shape
    band_width = stretch_rows + tap_count
    reversed_taps = filters[:, ::-1]
    pattern = jnp.concatenate(
        [
            jnp.zeros((groups, 1), filters.dtype),
            reversed_taps,
            jnp.zeros((groups, stretch_rows), filters.dtype),
        ],
        axis=1,
    )
    tiled = jnp.tile(pattern, (1, stretch_rows))[:, : stretch_rows * band_width]
    return tiled.reshape(groups, stretch_rows, band_width)


def band_sums(products, tap_count):
    groups, stretch_rows, band_width = products.shape
    flat_view = jnp.pad(
        products.reshape(groups, stretch_rows * band_width), ((0, 0), (0, stretch_rows))
    )
    folded = flat_view.reshape(groups, stretch_rows, band_width + 1).sum(axis=1)
    return folded[:, tap_count:0:-1]


def band_sums_ahead(products, tap_count):
    groups, stretch_rows, band_width = products.shape
    flat_view = jnp.pad(
        products.reshape(groups, stretch_rows * band_width), ((0, 0), (0, stretch_rows))
    )
    folded = flat_view.reshape(groups, stretch_rows, band_width + 1).sum(axis=1)
    return folded[:, :tap_count]


def body(tokens, w_in, gate, cotangent, filters):
    seq_count = tokens.shape[0]
    model_width = tokens.shape[3]
    channels = w_in.shape[2]
    groups, tap_count = filters.shape
    group_size = channels // groups
    stretch_rows = gate.shape[2]
    weight_flat = w_in.reshape(model_width, 2 * channels)
    inner = 4 if lax.axis_size("tensor") % 4 == 0 else 1
    block_rows = grid_gather(tokens.reshape(tokens.shape[2], model_width), "tensor", inner)
    projected = jnp.einsum(
        "nd,djc->njc", block_rows, w_in, preferred_element_type=jnp.float32
    ).astype(jnp.bfloat16).reshape(1, block_rows.shape[0], 2 * channels)
    second_in = projected[..., :channels].astype(jnp.float32)
    value_in = projected[..., channels:].astype(jnp.float32)
    mixed = (second_in * value_in).astype(jnp.bfloat16)
    gate_rows = gate[:, 0].astype(jnp.float32)
    grad_out = cotangent[:, 0].astype(jnp.float32)
    grad_mix = (grad_out * gate_rows).astype(jnp.bfloat16)
    prev_rows = from_behind(mixed[:, stretch_rows - (tap_count - 1) :], "context", 1)
    extended = jnp.concatenate(
        [jnp.zeros((seq_count, 1, channels), jnp.bfloat16), prev_rows, mixed], axis=1
    )
    extended = extended.reshape(seq_count, stretch_rows + tap_count, groups, group_size)
    toeplitz = skew_band(filters, stretch_rows)
    conv_out = jnp.einsum("gts,bsgc->btgc", toeplitz, extended, preferred_element_type=jnp.float32)
    conv_out = conv_out.reshape(seq_count, stretch_rows, channels)
    d_gate = (grad_out * conv_out).astype(jnp.bfloat16)[:, None]
    grad_blocks = grad_mix.reshape(seq_count, stretch_rows, groups, group_size)
    spread = jnp.einsum("gts,btgc->bsgc", toeplitz, grad_blocks, preferred_element_type=jnp.float32)
    own_part = spread[:, tap_count:]
    next_rows_in = from_behind(grad_mix[:, : tap_count - 1], "context", -1)
    next_blocks = next_rows_in.reshape(seq_count, tap_count - 1, groups, group_size)
    from_next = jnp.einsum(
        "gts,btgc->bsgc",
        toeplitz[:, : tap_count - 1, 1:tap_count],
        next_blocks,
        preferred_element_type=jnp.float32,
    )
    split_at = stretch_rows - tap_count + 1
    grad_conv = jnp.concatenate(
        [own_part[:, :split_at], own_part[:, split_at:] + from_next], axis=1
    )
    grad_conv = grad_conv.reshape(seq_count, stretch_rows, channels)
    grad_in = jnp.concatenate([grad_conv * value_in, grad_conv * second_in], axis=-1).astype(
        jnp.bfloat16
    )
    partials = jnp.einsum(
        "bnjc,djc->bnd",
        grad_in.reshape(grad_in.shape[:2] + (2, channels)),
        w_in,
        preferred_element_type=jnp.float32,
    )
    outer = lax.axis_size("tensor") // inner
    partial_rows = partials[0].astype(jnp.bfloat16)
    x_chunks = partial_rows.reshape((outer, -1) + partial_rows.shape[1:])
    grad_ahead = jnp.concatenate(
        [grad_mix, next_rows_in, jnp.zeros((seq_count, 1, channels), jnp.bfloat16)], axis=1
    ).reshape(seq_count, stretch_rows + tap_count, groups, group_size)
    products = jnp.einsum(
        "bsgc,btgc->gst",
        mixed.reshape(seq_count, stretch_rows, groups, group_size),
        grad_ahead,
        preferred_element_type=jnp.float32,
    )
    local_grad = band_sums_ahead(products, tap_count)
    if lax.axis_size("context") & (lax.axis_size("context") - 1) or lax.axis_size("dp") & (lax.axis_size("dp") - 1):
        summed = lax.psum(local_grad, ("context", "dp"))
        x_sums = scatter_stage(x_chunks, "tensor", inner, True, False)
        d_tokens = scatter_stage(x_sums.reshape((inner, -1) + x_sums.shape[1:]), "tensor", inner, False, True)
    else:
        context_steps = [1 << k for k in range(lax.axis_size("context").bit_length() - 1)]
        dp_steps = [1 << k for k in range(lax.axis_size("dp").bit_length() - 1)]
        first, second, third = context_steps[:1], context_steps[1:3], context_steps[3:]
        summed = butterfly_rounds(butterfly_rounds(local_grad, "dp", dp_steps), "context", first)
        x_sums = scatter_stage(x_chunks, "tensor", inner, True, False)
        x_sums, summed = lax.optimization_barrier((x_sums, summed))
        summed = butterfly_rounds(summed, "context", second)
        d_tokens = scatter_stage(x_sums.reshape((inner, -1) + x_sums.shape[1:]), "tensor", inner, False, True)
        d_tokens, summed = lax.optimization_barrier((d_tokens, summed))
        summed = butterfly_rounds(summed, "context", third)
    d_tokens = d_tokens.astype(jnp.bfloat16)[None, None]
    term_total = (
        seq_count * lax.axis_size("dp") * stretch_rows * lax.axis_size("context") * group_size
    )
    d_filter = summed * (1.0 / math.sqrt(term_total))
    return (d_tokens, d_gate, d_filter)


def solution(mesh):
    return jax.shard_map(
        body,
        mesh=mesh,
        in_specs=(
            P("dp", "context", "tensor", None),
            P(None, None, "tensor"),
            P("dp", "context", None, "tensor"),
            P("dp", "context", None, "tensor"),
            P("tensor", None),
        ),
        out_specs=(
            P("dp", "context", "tensor", None),
            P("dp", "context", None, "tensor"),
            P("tensor", None),
        ),
        check_vma=False,
    )
```

```python
import math

import jax
import jax.numpy as jnp
from jax import lax
from jax.sharding import PartitionSpec as P


def from_behind(value, axis, steps):
    count = lax.axis_size(axis)
    first, last = (max(0, -steps), min(count, count - steps))
    return lax.ppermute(value, axis, [(source, source + steps) for source in range(first, last)])


def butterfly_sum(value, axis):
    count = lax.axis_size(axis)
    if count & (count - 1):
        return lax.psum(value, axis)
    step = 1
    while step < count:
        value = value + lax.ppermute(value, axis, [(i, i ^ step) for i in range(count)])
        step *= 2
    return value


def butterfly_rounds(value, axis, steps):
    count = lax.axis_size(axis)
    for step in steps:
        value = value + lax.ppermute(value, axis, [(i, i ^ step) for i in range(count)])
    return value


def grid_shift(axis, steps, inner, outer_step):
    count = lax.axis_size(axis)
    if outer_step:
        return [(i, ((i // inner + steps) % (count // inner)) * inner + i % inner) for i in range(count)]
    return [(i, (i // inner) * inner + (i % inner + steps) % inner) for i in range(count)]


def grid_gather(rows, axis, inner):
    count = lax.axis_size(axis)
    outer = count // inner
    index = lax.axis_index(axis)
    pieces = [rows] + [
        lax.ppermute(rows, axis, grid_shift(axis, s, inner, False)) for s in range(1, inner)
    ]
    order = (index % inner - jnp.arange(inner)) % inner
    stage = jnp.take(jnp.stack(pieces), order, axis=0)
    pieces = [stage] + [
        lax.ppermute(stage, axis, grid_shift(axis, s, inner, True)) for s in range(1, outer)
    ]
    order = (index // inner - jnp.arange(outer)) % outer
    return jnp.take(jnp.stack(pieces), order, axis=0).reshape((count * rows.shape[0],) + rows.shape[1:])


def scatter_stage(chunks, axis, inner, outer_step, wide):
    count = lax.axis_size(axis)
    size = count // inner if outer_step else inner
    index = lax.axis_index(axis)
    place = index // inner if outer_step else index % inner
    acc = jnp.take(chunks, place, axis=0).astype(jnp.float32)
    for s in range(1, size):
        sent = jnp.take(chunks, (place + s) % size, axis=0)
        if wide:
            sent = sent.astype(jnp.float32)
        acc = acc + lax.ppermute(sent, axis, grid_shift(axis, s, inner, outer_step)).astype(jnp.float32)
    return acc


def skew_band(filters, stretch_rows):
    groups, tap_count = filters.shape
    band_width = stretch_rows + tap_count
    reversed_taps = filters[:, ::-1]
    pattern = jnp.concatenate(
        [
            jnp.zeros((groups, 1), filters.dtype),
            reversed_taps,
            jnp.zeros((groups, stretch_rows), filters.dtype),
        ],
        axis=1,
    )
    tiled = jnp.tile(pattern, (1, stretch_rows))[:, : stretch_rows * band_width]
    return tiled.reshape(groups, stretch_rows, band_width)


def band_sums(products, tap_count):
    groups, stretch_rows, band_width = products.shape
    flat_view = jnp.pad(
        products.reshape(groups, stretch_rows * band_width), ((0, 0), (0, stretch_rows))
    )
    folded = flat_view.reshape(groups, stretch_rows, band_width + 1).sum(axis=1)
    return folded[:, tap_count:0:-1]


def band_sums_ahead(products, tap_count):
    groups, stretch_rows, band_width = products.shape
    flat_view = jnp.pad(
        products.reshape(groups, stretch_rows * band_width), ((0, 0), (0, stretch_rows))
    )
    folded = flat_view.reshape(groups, stretch_rows, band_width + 1).sum(axis=1)
    return folded[:, :tap_count]


def body(tokens, w_in, gate, cotangent, filters):
    seq_count = tokens.shape[0]
    model_width = tokens.shape[3]
    channels = w_in.shape[2]
    groups, tap_count = filters.shape
    group_size = channels // groups
    stretch_rows = gate.shape[2]
    weight_flat = w_in.reshape(model_width, 2 * channels)
    inner = 4 if lax.axis_size("tensor") % 4 == 0 else 1
    block_rows = grid_gather(tokens.reshape(tokens.shape[2], model_width), "tensor", inner)
    projected = jnp.einsum(
        "nd,djc->njc", block_rows, w_in, preferred_element_type=jnp.float32
    ).astype(jnp.bfloat16).reshape(1, block_rows.shape[0], 2 * channels)
    second_in = projected[..., :channels].astype(jnp.float32)
    value_in = projected[..., channels:].astype(jnp.float32)
    mixed = (second_in * value_in).astype(jnp.bfloat16)
    gate_rows = gate[:, 0].astype(jnp.float32)
    grad_out = cotangent[:, 0].astype(jnp.float32)
    grad_mix = (grad_out * gate_rows).astype(jnp.bfloat16)
    prev_rows = from_behind(mixed[:, stretch_rows - (tap_count - 1) :], "context", 1)
    extended = jnp.concatenate(
        [jnp.zeros((seq_count, 1, channels), jnp.bfloat16), prev_rows, mixed], axis=1
    )
    extended = extended.reshape(seq_count, stretch_rows + tap_count, groups, group_size)
    toeplitz = skew_band(filters, stretch_rows)
    conv_out = jnp.einsum("gts,bsgc->btgc", toeplitz, extended, preferred_element_type=jnp.float32)
    conv_out = conv_out.reshape(seq_count, stretch_rows, channels)
    d_gate = (grad_out * conv_out).astype(jnp.bfloat16)[:, None]
    grad_blocks = grad_mix.reshape(seq_count, stretch_rows, groups, group_size)
    spread = jnp.einsum("gts,btgc->bsgc", toeplitz, grad_blocks, preferred_element_type=jnp.float32)
    own_part = spread[:, tap_count:]
    next_rows_in = from_behind(grad_mix[:, : tap_count - 1], "context", -1)
    next_blocks = next_rows_in.reshape(seq_count, tap_count - 1, groups, group_size)
    from_next = jnp.einsum(
        "gts,btgc->bsgc",
        toeplitz[:, : tap_count - 1, 1:tap_count],
        next_blocks,
        preferred_element_type=jnp.float32,
    )
    split_at = stretch_rows - tap_count + 1
    grad_conv = jnp.concatenate(
        [own_part[:, :split_at], own_part[:, split_at:] + from_next], axis=1
    )
    grad_conv = grad_conv.reshape(seq_count, stretch_rows, channels)
    grad_in = jnp.concatenate([grad_conv * value_in, grad_conv * second_in], axis=-1).astype(
        jnp.bfloat16
    )

    def row_chunks(grad_in):
        partials = jnp.einsum(
            "bnjc,djc->bnd",
            grad_in.reshape(grad_in.shape[:2] + (2, channels)),
            w_in,
            preferred_element_type=jnp.float32,
        )
        partial_rows = partials[0].astype(jnp.bfloat16)
        return partial_rows.reshape((outer, -1) + partial_rows.shape[1:])

    outer = lax.axis_size("tensor") // inner
    grad_ahead = jnp.concatenate(
        [grad_mix, next_rows_in, jnp.zeros((seq_count, 1, channels), jnp.bfloat16)], axis=1
    ).reshape(seq_count, stretch_rows + tap_count, groups, group_size)
    products = jnp.einsum(
        "bsgc,btgc->gst",
        mixed.reshape(seq_count, stretch_rows, groups, group_size),
        grad_ahead,
        preferred_element_type=jnp.float32,
    )
    local_grad = band_sums_ahead(products, tap_count)
    if lax.axis_size("context") & (lax.axis_size("context") - 1) or lax.axis_size("dp") & (lax.axis_size("dp") - 1):
        summed = lax.psum(local_grad, ("context", "dp"))
        x_chunks = row_chunks(grad_in)
        x_sums = scatter_stage(x_chunks, "tensor", inner, True, False)
        d_tokens = scatter_stage(x_sums.reshape((inner, -1) + x_sums.shape[1:]), "tensor", inner, False, True)
    else:
        context_steps = [1 << k for k in range(lax.axis_size("context").bit_length() - 1)]
        dp_steps = [1 << k for k in range(lax.axis_size("dp").bit_length() - 1)]
        first, second, third = context_steps[:1], context_steps[1:3], context_steps[3:]
        summed = butterfly_rounds(local_grad, "dp", dp_steps)
        grad_in, summed = lax.optimization_barrier((grad_in, summed))
        summed = butterfly_rounds(summed, "context", first)
        x_chunks = row_chunks(grad_in)
        x_sums = scatter_stage(x_chunks, "tensor", inner, True, False)
        x_sums, summed = lax.optimization_barrier((x_sums, summed))
        summed = butterfly_rounds(summed, "context", second)
        d_tokens = scatter_stage(x_sums.reshape((inner, -1) + x_sums.shape[1:]), "tensor", inner, False, True)
        d_tokens, summed = lax.optimization_barrier((d_tokens, summed))
        summed = butterfly_rounds(summed, "context", third)
    d_tokens = d_tokens.astype(jnp.bfloat16)[None, None]
    term_total = (
        seq_count * lax.axis_size("dp") * stretch_rows * lax.axis_size("context") * group_size
    )
    d_filter = summed * (1.0 / math.sqrt(term_total))
    return (d_tokens, d_gate, d_filter)


def solution(mesh):
    return jax.shard_map(
        body,
        mesh=mesh,
        in_specs=(
            P("dp", "context", "tensor", None),
            P(None, None, "tensor"),
            P("dp", "context", None, "tensor"),
            P("dp", "context", None, "tensor"),
            P("tensor", None),
        ),
        out_specs=(
            P("dp", "context", "tensor", None),
            P("dp", "context", None, "tensor"),
            P("tensor", None),
        ),
        check_vma=False,
    )
```

```python
import math

import jax
import jax.numpy as jnp
from jax import lax
from jax.sharding import PartitionSpec as P


def from_behind(value, axis, steps):
    count = lax.axis_size(axis)
    first, last = (max(0, -steps), min(count, count - steps))
    return lax.ppermute(value, axis, [(source, source + steps) for source in range(first, last)])


def butterfly_sum(value, axis):
    count = lax.axis_size(axis)
    if count & (count - 1):
        return lax.psum(value, axis)
    step = 1
    while step < count:
        value = value + lax.ppermute(value, axis, [(i, i ^ step) for i in range(count)])
        step *= 2
    return value


def butterfly_rounds(value, axis, steps):
    count = lax.axis_size(axis)
    for step in steps:
        value = value + lax.ppermute(value, axis, [(i, i ^ step) for i in range(count)])
    return value


def grid_shift(axis, steps, inner, outer_step):
    count = lax.axis_size(axis)
    if outer_step:
        return [(i, ((i // inner + steps) % (count // inner)) * inner + i % inner) for i in range(count)]
    return [(i, (i // inner) * inner + (i % inner + steps) % inner) for i in range(count)]


def grid_gather(rows, axis, inner):
    count = lax.axis_size(axis)
    outer = count // inner
    index = lax.axis_index(axis)
    pieces = [rows] + [
        lax.ppermute(rows, axis, grid_shift(axis, s, inner, False)) for s in range(1, inner)
    ]
    order = (index % inner - jnp.arange(inner)) % inner
    stage = jnp.take(jnp.stack(pieces), order, axis=0)
    pieces = [stage] + [
        lax.ppermute(stage, axis, grid_shift(axis, s, inner, True)) for s in range(1, outer)
    ]
    order = (index // inner - jnp.arange(outer)) % outer
    return jnp.take(jnp.stack(pieces), order, axis=0).reshape((count * rows.shape[0],) + rows.shape[1:])


def scatter_stage(chunks, axis, inner, outer_step, wide):
    count = lax.axis_size(axis)
    size = count // inner if outer_step else inner
    index = lax.axis_index(axis)
    place = index // inner if outer_step else index % inner
    acc = jnp.take(chunks, place, axis=0).astype(jnp.float32)
    for s in range(1, size):
        sent = jnp.take(chunks, (place + s) % size, axis=0)
        if wide:
            sent = sent.astype(jnp.float32)
        acc = acc + lax.ppermute(sent, axis, grid_shift(axis, s, inner, outer_step)).astype(jnp.float32)
    return acc


def skew_band(filters, stretch_rows):
    groups, tap_count = filters.shape
    band_width = stretch_rows + tap_count
    reversed_taps = filters[:, ::-1]
    pattern = jnp.concatenate(
        [
            jnp.zeros((groups, 1), filters.dtype),
            reversed_taps,
            jnp.zeros((groups, stretch_rows), filters.dtype),
        ],
        axis=1,
    )
    tiled = jnp.tile(pattern, (1, stretch_rows))[:, : stretch_rows * band_width]
    return tiled.reshape(groups, stretch_rows, band_width)


def band_sums(products, tap_count):
    groups, stretch_rows, band_width = products.shape
    flat_view = jnp.pad(
        products.reshape(groups, stretch_rows * band_width), ((0, 0), (0, stretch_rows))
    )
    folded = flat_view.reshape(groups, stretch_rows, band_width + 1).sum(axis=1)
    return folded[:, tap_count:0:-1]


def band_sums_ahead(products, tap_count):
    groups, stretch_rows, band_width = products.shape
    flat_view = jnp.pad(
        products.reshape(groups, stretch_rows * band_width), ((0, 0), (0, stretch_rows))
    )
    folded = flat_view.reshape(groups, stretch_rows, band_width + 1).sum(axis=1)
    return folded[:, :tap_count]


def body(tokens, w_in, gate, cotangent, filters):
    seq_count = tokens.shape[0]
    model_width = tokens.shape[3]
    channels = w_in.shape[2]
    groups, tap_count = filters.shape
    group_size = channels // groups
    stretch_rows = gate.shape[2]
    weight_flat = w_in.reshape(model_width, 2 * channels)
    inner = 4 if lax.axis_size("tensor") % 4 == 0 else 1
    block_rows = grid_gather(tokens.reshape(tokens.shape[2], model_width), "tensor", inner)
    projected = jnp.einsum(
        "nd,djc->njc", block_rows, w_in, preferred_element_type=jnp.float32
    ).astype(jnp.bfloat16).reshape(1, block_rows.shape[0], 2 * channels)
    second_in = projected[..., :channels].astype(jnp.float32)
    value_in = projected[..., channels:].astype(jnp.float32)
    mixed = (second_in * value_in).astype(jnp.bfloat16)
    gate_rows = gate[:, 0].astype(jnp.float32)
    grad_out = cotangent[:, 0].astype(jnp.float32)
    grad_mix = (grad_out * gate_rows).astype(jnp.bfloat16)
    prev_rows = from_behind(mixed[:, stretch_rows - (tap_count - 1) :], "context", 1)
    extended = jnp.concatenate(
        [jnp.zeros((seq_count, 1, channels), jnp.bfloat16), prev_rows, mixed], axis=1
    )
    extended = extended.reshape(seq_count, stretch_rows + tap_count, groups, group_size)
    toeplitz = skew_band(filters, stretch_rows)
    conv_out = jnp.einsum("gts,bsgc->btgc", toeplitz, extended, preferred_element_type=jnp.float32)
    conv_out = conv_out.reshape(seq_count, stretch_rows, channels)
    d_gate = (grad_out * conv_out).astype(jnp.bfloat16)[:, None]
    grad_blocks = grad_mix.reshape(seq_count, stretch_rows, groups, group_size)
    spread = jnp.einsum("gts,btgc->bsgc", toeplitz, grad_blocks, preferred_element_type=jnp.float32)
    own_part = spread[:, tap_count:]
    next_rows_in = from_behind(grad_mix[:, : tap_count - 1], "context", -1)
    next_blocks = next_rows_in.reshape(seq_count, tap_count - 1, groups, group_size)
    from_next = jnp.einsum(
        "gts,btgc->bsgc",
        toeplitz[:, : tap_count - 1, 1:tap_count],
        next_blocks,
        preferred_element_type=jnp.float32,
    )
    split_at = stretch_rows - tap_count + 1
    grad_conv = jnp.concatenate(
        [own_part[:, :split_at], own_part[:, split_at:] + from_next], axis=1
    )
    grad_conv = grad_conv.reshape(seq_count, stretch_rows, channels)
    grad_in = jnp.concatenate([grad_conv * value_in, grad_conv * second_in], axis=-1).astype(
        jnp.bfloat16
    )
    partials = jnp.einsum(
        "bnjc,djc->bnd",
        grad_in.reshape(grad_in.shape[:2] + (2, channels)),
        w_in,
        preferred_element_type=jnp.float32,
    )
    outer = lax.axis_size("tensor") // inner
    partial_rows = partials[0].astype(jnp.bfloat16)
    x_chunks = partial_rows.reshape((outer, -1) + partial_rows.shape[1:])
    grad_ahead = jnp.concatenate(
        [grad_mix, next_rows_in, jnp.zeros((seq_count, 1, channels), jnp.bfloat16)], axis=1
    ).reshape(seq_count, stretch_rows + tap_count, groups, group_size)
    products = jnp.einsum(
        "bsgc,btgc->gst",
        mixed.reshape(seq_count, stretch_rows, groups, group_size),
        grad_ahead,
        preferred_element_type=jnp.float32,
    )
    local_grad = band_sums_ahead(products, tap_count)
    if lax.axis_size("context") & (lax.axis_size("context") - 1) or lax.axis_size("dp") & (lax.axis_size("dp") - 1):
        summed = lax.psum(local_grad, ("context", "dp"))
        x_sums = scatter_stage(x_chunks, "tensor", inner, True, False)
        d_tokens = scatter_stage(x_sums.reshape((inner, -1) + x_sums.shape[1:]), "tensor", inner, False, True)
    else:
        context_steps = [1 << k for k in range(lax.axis_size("context").bit_length() - 1)]
        dp_steps = [1 << k for k in range(lax.axis_size("dp").bit_length() - 1)]
        context_steps = context_steps[::-1]
        first, second, third = context_steps[:2], context_steps[2:4], context_steps[4:]
        summed = butterfly_rounds(butterfly_rounds(local_grad, "dp", dp_steps), "context", first)
        x_sums = scatter_stage(x_chunks, "tensor", inner, True, False)
        x_sums, summed = lax.optimization_barrier((x_sums, summed))
        summed = butterfly_rounds(summed, "context", second)
        d_tokens = scatter_stage(x_sums.reshape((inner, -1) + x_sums.shape[1:]), "tensor", inner, False, True)
        d_tokens, summed = lax.optimization_barrier((d_tokens, summed))
        summed = butterfly_rounds(summed, "context", third)
    d_tokens = d_tokens.astype(jnp.bfloat16)[None, None]
    term_total = (
        seq_count * lax.axis_size("dp") * stretch_rows * lax.axis_size("context") * group_size
    )
    d_filter = summed * (1.0 / math.sqrt(term_total))
    return (d_tokens, d_gate, d_filter)


def solution(mesh):
    return jax.shard_map(
        body,
        mesh=mesh,
        in_specs=(
            P("dp", "context", "tensor", None),
            P(None, None, "tensor"),
            P("dp", "context", None, "tensor"),
            P("dp", "context", None, "tensor"),
            P("tensor", None),
        ),
        out_specs=(
            P("dp", "context", "tensor", None),
            P("dp", "context", None, "tensor"),
            P("tensor", None),
        ),
        check_vma=False,
    )
```
